128 devices in a mesh: row: 8 (over x_lo, z), col: 16 (over y, x_hi, core).
Axes of the slice: x: 4 (x_hi: 2, x_lo: 2; x = x_hi * 2 + x_lo), y: 4, z: 4, core: 2. Of those that a mesh axis runs over, the one named last changes fastest.
Arguments:
- amplitudes: bfloat16 [768, 640000], P('col', 'row'), may hold values from -6 to 6
- integrals: bfloat16 [640000, 1600], P(('row', 'col')), may hold values from -0.0078125 to 0.0078125
- occ_irrep: int32 [120], replicated, may hold values from 0 to 7, as said below
- vir_irrep: int32 [800], replicated, may hold values from 0 to 7, as said below
- tile_owner: int32 [384], replicated, may hold values from 0 to 127, as said below
Outputs:
- inbox: bfloat16 [1536, 1600], P(('row', 'col'))
The draws below stay inside these ranges and needn't reach their ends.
Inputs may be any that keep to these rules, and one draw needn't show every extreme that they name: `tile_owner`: no device owns more than 6 tiles and some device owns exactly 6; in every draw the 3 tiles of some device's rows of result all have one owner. `occ_irrep`: labels never decrease along the orbitals, so each irrep's orbitals form one contiguous block. Each of irreps 1 to 7 holds at least one and at most 2 orbitals, one of them exactly that most; irrep 0 holds all the others. `vir_irrep`: labels never decrease along the orbitals, so each irrep's orbitals form one contiguous block. Each of irreps 1 to 7 holds at least one and at most 13 orbitals, one of them exactly that most; irrep 0 holds all the others.
All inputs are finite; a program needn't handle non-finite values.
Results may differ from the reference program's by a relative error of at most 0.0014.
Values may be sent and summed in bfloat16 or wider, within the bound.
No kernel may reach another device: no remote copies, remote signals or barrier semaphores. Data moves between devices by JAX's collectives and lax.ppermute only.
A program may use at most 192 MiB of HBM per device.

```python
import jax
import jax.numpy as jnp
from jax import lax

NO = 120
NV = 800
TR = 2
PAIRS = 768
CD = 640000
AB = 1600
TILES_DEV = 3
NT = 384
CAP = 6
N_ROW = 8
N_COL = 16
DEVICES = 128


def sorted_labels(key, count):
    minor_most = max(2, count // 60)
    keys = jax.random.split(key, 2)
    minor_sizes = jax.random.randint(keys[0], (7,), 1, minor_most + 1).astype(jnp.int32)
    fullest = jax.random.randint(keys[1], (), 0, 7).astype(jnp.int32)
    minor_sizes = jnp.where(jnp.arange(7, dtype=jnp.int32) == fullest, jnp.int32(minor_most), minor_sizes).astype(jnp.int32)
    running = jnp.cumsum(minor_sizes).astype(jnp.int32)
    minor_total = running[6]
    offsets = jnp.concatenate([jnp.zeros((1,), jnp.int32), running[:6]])
    starts = (count - minor_total + offsets).astype(jnp.int32)
    positions = jnp.arange(count, dtype=jnp.int32)
    return jnp.sum((positions[:, None] >= starts[None, :]).astype(jnp.int32), axis=1).astype(jnp.int32)


def draw_occ_irrep(key, part):
    return sorted_labels(jax.random.fold_in(key, 31), NO)


def draw_vir_irrep(key, part):
    return sorted_labels(jax.random.fold_in(key, 47), NV)


def draw_tile_owner(key, part):
    keys = jax.random.split(jax.random.fold_in(key, 17), 4)
    target = jax.random.randint(keys[0], (), 0, DEVICES).astype(jnp.int32)
    source = jax.random.randint(keys[1], (), 0, DEVICES).astype(jnp.int32)
    others = (jax.random.permutation(keys[2], DEVICES * CAP - CAP)[:NT - CAP] // CAP).astype(jnp.int32)
    others = others + (others >= target).astype(jnp.int32)
    labels = jnp.concatenate([jnp.full((CAP,), target, jnp.int32), others])
    remain = jax.random.permutation(keys[3], NT - TILES_DEV).astype(jnp.int32)
    remain = remain + TILES_DEV * (remain >= source * TILES_DEV).astype(jnp.int32)
    order = jnp.concatenate([source * TILES_DEV + jnp.arange(TILES_DEV, dtype=jnp.int32), remain])
    return jnp.zeros((NT,), jnp.int32).at[order].set(labels)


def raised(values, rng, source, target, blocks, factor):
    def block_of(axis_at):
        return (jnp.arange(values.shape[axis_at]) // (values.shape[axis_at] // blocks)).reshape((-1,) + (1,) * (values.ndim - 1 - axis_at))

    first = jax.random.permutation(rng, blocks)[block_of(target)]
    far = (block_of(target) + blocks // 2) % blocks
    return jnp.where((block_of(source) == first) | (block_of(source) == far), factor * values, values)


def steps_of(key, extent, cuts, low, largest):
    factor_of = 1.0
    for axis_at, shards_of in cuts:
        draws = jax.random.uniform(jax.random.fold_in(jax.random.fold_in(key, 6), axis_at), (shards_of,), jnp.float32, low / len(cuts), largest / len(cuts))
        factor_of = factor_of * jnp.repeat(jnp.exp(draws), extent[axis_at] // shards_of).reshape((-1,) + (1,) * (len(extent) - 1 - axis_at))
    return factor_of


def centred(rng, extent, scale, reach, cuts=(), kind=jnp.bfloat16):
    level = steps_of(rng, extent, cuts, -0.22, 0.18) if cuts else 1.0
    values = jax.random.normal(rng, extent, jnp.float32) * scale * level
    return jnp.minimum(jnp.maximum(values, -reach), reach).astype(kind)


def gaussian_with(key, extent, width, reach, cuts, heavy, kind=jnp.bfloat16):
    array = width * jax.random.normal(key, extent, jnp.float32)
    if cuts:
        array = array * steps_of(key, extent, cuts, -0.22, 0.18)
    return jnp.clip(raised(array, jax.random.fold_in(key, 3), *heavy), -reach, reach).astype(kind)


def setup_inputs(seed: int = 0) -> dict:
    streams_of = jax.random.split(jax.random.key(seed), 6)
    amplitudes = gaussian_with(streams_of[0], (PAIRS, CD), 1.0, 6.0, ((0, 16), (1, 8)), (1, 0, 16, 2.0))
    integrals = centred(streams_of[1], (CD, AB), CD ** -0.5, 0.0078125, ((0, 128),))
    occ_irrep = draw_occ_irrep(jax.random.fold_in(streams_of[5], 71), 0)
    vir_irrep = draw_vir_irrep(jax.random.fold_in(streams_of[5], 71), 0)
    tile_owner = draw_tile_owner(jax.random.fold_in(streams_of[5], 71), 0)
    return {"amplitudes": amplitudes, "integrals": integrals, "occ_irrep": occ_irrep, "vir_irrep": vir_irrep, "tile_owner": tile_owner}


def reference(amplitudes, integrals, occ_irrep, vir_irrep, tile_owner):
    pair_index = jnp.arange(PAIRS, dtype=jnp.int32)
    pair_irrep = jnp.bitwise_xor(occ_irrep[pair_index // NO], occ_irrep[pair_index % NO])
    ab_index = jnp.arange(AB, dtype=jnp.int32)
    ab_irrep = jnp.bitwise_xor(vir_irrep[ab_index // NV], vir_irrep[ab_index % NV])

    def accumulate(block, total):
        cd_irrep = jnp.bitwise_xor(vir_irrep[block], vir_irrep)
        start = (block * NV).astype(jnp.int32)
        panel = lax.dynamic_slice(amplitudes, (jnp.int32(0), start), (PAIRS, NV)).astype(jnp.float32)
        slab = lax.dynamic_slice(integrals, (start, jnp.int32(0)), (NV, AB)).astype(jnp.float32)
        masked_t = jnp.where(pair_irrep[:, None] == cd_irrep[None, :], panel, jnp.zeros((), jnp.float32))
        masked_v = jnp.where(cd_irrep[:, None] == ab_irrep[None, :], slab, jnp.zeros((), jnp.float32))
        return total + jnp.dot(masked_t, masked_v, precision=lax.Precision.HIGHEST)

    total = lax.fori_loop(0, NV, accumulate, jnp.zeros((PAIRS, AB), jnp.float32))
    result = total.astype(jnp.bfloat16)
    tiles = result.reshape(NT, TR * AB)
    tile_ids = jnp.arange(NT, dtype=jnp.int32)
    same = tile_owner[:, None] == tile_owner[None, :]
    earlier = tile_ids[:, None] > tile_ids[None, :]
    rank = jnp.sum(jnp.where(same & earlier, 1, 0), axis=1).astype(jnp.int32)
    slot = (tile_owner * CAP + rank).astype(jnp.int32)
    inbox = jnp.zeros((N_ROW * N_COL * CAP, TR * AB), jnp.bfloat16).at[slot].set(tiles)
    return inbox.reshape(N_ROW * N_COL * CAP * TR, AB)
```

```python
import jax
import jax.numpy as jnp
from jax import lax
from jax.sharding import PartitionSpec as P

TR = 2
TILES_DEV = 3
CAP = 6


def lookup(table, index):
    entries = table.shape[0]
    hits = index[:, None] == jnp.arange(entries, dtype=jnp.int32)[None, :]
    return jnp.sum(jnp.where(hits, table[None, :], 0), axis=1)


def on_device(amplitudes, integrals, occ_irrep, vir_irrep, tile_owner):
    ncols = lax.axis_size("col")
    nrows = lax.axis_size("row")
    devices = nrows * ncols
    myself = lax.axis_index("row") * ncols + lax.axis_index("col")
    cd_dev = integrals.shape[0]
    ab_width = integrals.shape[1]
    local_pairs = amplitudes.shape[0]
    pair_count = local_pairs * ncols
    norb = occ_irrep.shape[0]
    nvirt = vir_irrep.shape[0]
    pair_index = jnp.arange(pair_count, dtype=jnp.int32)
    pair_irrep = jnp.bitwise_xor(
        lookup(occ_irrep, pair_index // norb), lookup(occ_irrep, pair_index % norb)
    )
    ab_index = jnp.arange(ab_width, dtype=jnp.int32)
    ab_irrep = jnp.bitwise_xor(
        lookup(vir_irrep, ab_index // nvirt), lookup(vir_irrep, ab_index % nvirt)
    )
    zero_half = jnp.zeros((), jnp.bfloat16)
    panel = lax.all_to_all(amplitudes, "col", split_axis=1, concat_axis=0, tiled=True)
    width = panel.shape[1]
    cd_index = myself * cd_dev + jnp.arange(width, dtype=jnp.int32)
    cd_irrep = jnp.bitwise_xor(
        lookup(vir_irrep, cd_index // nvirt), lookup(vir_irrep, cd_index % nvirt)
    )
    masked_t = jnp.where(pair_irrep[:, None] == cd_irrep[None, :], panel, zero_half)
    masked_v = jnp.where(cd_irrep[:, None] == ab_irrep[None, :], integrals, zero_half)
    ntiles = tile_owner.shape[0]
    tile_ids = jnp.arange(ntiles, dtype=jnp.int32)
    same = tile_owner[:, None] == tile_owner[None, :]
    earlier = tile_ids[:, None] > tile_ids[None, :]
    rank = jnp.sum(jnp.where(same & earlier, 1, 0), axis=1).astype(jnp.int32)
    slot = tile_owner * CAP + rank
    total = jnp.dot(masked_t, masked_v, preferred_element_type=jnp.float32)
    chunk = total.size // devices
    flat = total.reshape(devices, chunk // 128, 128)
    summed = lax.psum_scatter(flat, ("row", "col"), scatter_dimension=0, tiled=True)
    my_tiles = summed.astype(jnp.bfloat16).reshape(TILES_DEV, TR * ab_width)
    every = lax.all_gather(my_tiles, ("row", "col"), axis=0, tiled=True)
    wanted = myself * CAP + jnp.arange(CAP, dtype=jnp.int32)
    match = slot[None, :] == wanted[:, None]
    source = jnp.sum(jnp.where(match, tile_ids[None, :], 0), axis=1)
    found = jnp.any(match, axis=1)
    picked = jnp.take(every, source, axis=0)
    placed = jnp.where(found[:, None], picked, zero_half)
    return placed.reshape(CAP * TR, ab_width)


def solution(mesh):
    in_specs = (P("col", "row"), P(("row", "col"), None), P(), P(), P())
    out_specs = P(("row", "col"), None)
    return jax.shard_map(
        on_device, mesh=mesh, in_specs=in_specs, out_specs=out_specs, check_vma=False
    )
```

```python
import jax
import jax.numpy as jnp
from jax import lax
from jax.sharding import PartitionSpec as P

TR = 2
TILES_DEV = 3
CAP = 6


def lookup(table, index):
    entries = table.shape[0]
    hits = index[:, None] == jnp.arange(entries, dtype=jnp.int32)[None, :]
    return jnp.sum(jnp.where(hits, table[None, :], 0), axis=1)


def on_device(amplitudes, integrals, occ_irrep, vir_irrep, tile_owner):
    ncols = lax.axis_size("col")
    nrows = lax.axis_size("row")
    devices = nrows * ncols
    myself = lax.axis_index("row") * ncols + lax.axis_index("col")
    cd_dev = integrals.shape[0]
    ab_width = integrals.shape[1]
    local_pairs = amplitudes.shape[0]
    pair_count = local_pairs * ncols
    norb = occ_irrep.shape[0]
    nvirt = vir_irrep.shape[0]
    pair_index = jnp.arange(pair_count, dtype=jnp.int32)
    pair_irrep = jnp.bitwise_xor(
        lookup(occ_irrep, pair_index // norb), lookup(occ_irrep, pair_index % norb)
    )
    ab_index = jnp.arange(ab_width, dtype=jnp.int32)
    ab_irrep = jnp.bitwise_xor(
        lookup(vir_irrep, ab_index // nvirt), lookup(vir_irrep, ab_index % nvirt)
    )
    zero_half = jnp.zeros((), jnp.bfloat16)
    panel = lax.all_to_all(amplitudes, "col", split_axis=1, concat_axis=0, tiled=True)
    width = panel.shape[1]
    cd_index = myself * cd_dev + jnp.arange(width, dtype=jnp.int32)
    cd_irrep = jnp.bitwise_xor(
        lookup(vir_irrep, cd_index // nvirt), lookup(vir_irrep, cd_index % nvirt)
    )
    masked_t = jnp.where(pair_irrep[:, None] == cd_irrep[None, :], panel, zero_half)
    masked_v = jnp.where(cd_irrep[:, None] == ab_irrep[None, :], integrals, zero_half)
    ntiles = tile_owner.shape[0]
    tile_ids = jnp.arange(ntiles, dtype=jnp.int32)
    same = tile_owner[:, None] == tile_owner[None, :]
    earlier = tile_ids[:, None] > tile_ids[None, :]
    rank = jnp.sum(jnp.where(same & earlier, 1, 0), axis=1).astype(jnp.int32)
    slot = tile_owner * CAP + rank
    total = jnp.dot(masked_t, masked_v, preferred_element_type=jnp.float32)
    summed = lax.psum(total, ("row", "col"))
    every = summed.reshape(ntiles, TR * ab_width)
    wanted = myself * CAP + jnp.arange(CAP, dtype=jnp.int32)
    match = slot[None, :] == wanted[:, None]
    source = jnp.sum(jnp.where(match, tile_ids[None, :], 0), axis=1)
    found = jnp.any(match, axis=1)
    picked = jnp.take(every, source, axis=0).astype(jnp.bfloat16)
    placed = jnp.where(found[:, None], picked, zero_half)
    return placed.reshape(CAP * TR, ab_width)


def solution(mesh):
    in_specs = (P("col", "row"), P(("row", "col"), None), P(), P(), P())
    out_specs = P(("row", "col"), None)
    return jax.shard_map(
        on_device, mesh=mesh, in_specs=in_specs, out_specs=out_specs, check_vma=False
    )
```

```python
import jax
import jax.numpy as jnp
from jax import lax
from jax.sharding import PartitionSpec as P

TR = 2
TILES_DEV = 3
CAP = 6
PIECES = 2


def lookup(table, index):
    return jnp.take(table, index, axis=0, mode="clip")


def on_device(amplitudes, integrals, occ_irrep, vir_irrep, tile_owner):
    ncols = lax.axis_size("col")
    nrows = lax.axis_size("row")
    myself = lax.axis_index("row") * ncols + lax.axis_index("col")
    cd_dev = integrals.shape[0]
    ab_width = integrals.shape[1]
    local_pairs = amplitudes.shape[0]
    pair_count = local_pairs * ncols
    norb = occ_irrep.shape[0]
    nvirt = vir_irrep.shape[0]
    pair_index = jnp.arange(pair_count, dtype=jnp.int32)
    pair_irrep = jnp.bitwise_xor(
        lookup(occ_irrep, pair_index // norb), lookup(occ_irrep, pair_index % norb)
    )
    ab_index = jnp.arange(ab_width, dtype=jnp.int32)
    ab_irrep = jnp.bitwise_xor(
        lookup(vir_irrep, ab_index // nvirt), lookup(vir_irrep, ab_index % nvirt)
    )
    zero_half = jnp.zeros((), jnp.bfloat16)
    piece = cd_dev // PIECES
    split = amplitudes.reshape(local_pairs, ncols, PIECES, piece)
    total = None
    for h in range(PIECES):
        part = split[:, :, h, :].reshape(local_pairs, ncols * piece)
        panel = lax.all_to_all(part, "col", split_axis=1, concat_axis=0, tiled=True)
        cd_index = myself * cd_dev + h * piece + jnp.arange(piece, dtype=jnp.int32)
        cd_irrep = jnp.bitwise_xor(
            lookup(vir_irrep, cd_index // nvirt), lookup(vir_irrep, cd_index % nvirt)
        )
        slab = integrals[h * piece:(h + 1) * piece]
        masked_t = jnp.where(pair_irrep[:, None] == cd_irrep[None, :], panel, zero_half)
        masked_v = jnp.where(cd_irrep[:, None] == ab_irrep[None, :], slab, zero_half)
        term = jnp.dot(masked_t, masked_v, preferred_element_type=jnp.float32)
        total = term if total is None else total + term
    ntiles = tile_owner.shape[0]
    tile_ids = jnp.arange(ntiles, dtype=jnp.int32)
    same = tile_owner[:, None] == tile_owner[None, :]
    earlier = tile_ids[:, None] > tile_ids[None, :]
    rank = jnp.sum(jnp.where(same & earlier, 1, 0), axis=1).astype(jnp.int32)
    slot = tile_owner * CAP + rank
    summed = lax.psum(total, ("row", "col"))
    wanted = myself * CAP + jnp.arange(CAP, dtype=jnp.int32)
    match = slot[None, :] == wanted[:, None]
    source = jnp.sum(jnp.where(match, tile_ids[None, :], 0), axis=1)
    found = jnp.any(match, axis=1)
    rows = (source[:, None] * TR + jnp.arange(TR, dtype=jnp.int32)[None, :]).reshape(CAP * TR)
    keep = jnp.repeat(found, TR)
    picked = jnp.take(summed, rows, axis=0).astype(jnp.bfloat16)
    placed = jnp.where(keep[:, None], picked, zero_half)
    return placed.reshape(CAP * TR, ab_width)


def solution(mesh):
    in_specs = (P("col", "row"), P(("row", "col"), None), P(), P(), P())
    out_specs = P(("row", "col"), None)
    return jax.shard_map(
        on_device, mesh=mesh, in_specs=in_specs, out_specs=out_specs, check_vma=False
    )
```

```python
import jax
import jax.numpy as jnp
from jax import lax
from jax.sharding import PartitionSpec as P

TR = 2
TILES_DEV = 3
CAP = 6
PIECES = 2


def lookup(table, index):
    levels = jnp.arange(1, 8, dtype=jnp.int32)
    starts = jnp.sum((table[None, :] < levels[:, None]).astype(jnp.int32), axis=1)
    return jnp.sum((index[:, None] >= starts[None, :]).astype(jnp.int32), axis=1)


def on_device(amplitudes, integrals, occ_irrep, vir_irrep, tile_owner):
    ncols = lax.axis_size("col")
    nrows = lax.axis_size("row")
    myself = lax.axis_index("row") * ncols + lax.axis_index("col")
    cd_dev = integrals.shape[0]
    ab_width = integrals.shape[1]
    local_pairs = amplitudes.shape[0]
    norb = occ_irrep.shape[0]
    nvirt = vir_irrep.shape[0]
    ab_index = jnp.arange(ab_width, dtype=jnp.int32)
    ab_irrep = jnp.bitwise_xor(
        lookup(vir_irrep, ab_index // nvirt), lookup(vir_irrep, ab_index % nvirt)
    )
    zero_half = jnp.zeros((), jnp.bfloat16)
    cd_index = myself * cd_dev + jnp.arange(cd_dev, dtype=jnp.int32)
    cd_irrep = jnp.bitwise_xor(
        lookup(vir_irrep, cd_index // nvirt), lookup(vir_irrep, cd_index % nvirt)
    )
    masked_v = jnp.where(cd_irrep[:, None] == ab_irrep[None, :], integrals, zero_half)
    rows_piece = local_pairs // PIECES
    terms = []
    for h in range(PIECES):
        part = amplitudes[h * rows_piece:(h + 1) * rows_piece]
        panel = lax.all_to_all(part, "col", split_axis=1, concat_axis=0, tiled=True)
        piece_pairs = (
            jnp.arange(ncols, dtype=jnp.int32)[:, None] * local_pairs
            + h * rows_piece
            + jnp.arange(rows_piece, dtype=jnp.int32)[None, :]
        ).reshape(ncols * rows_piece)
        piece_irrep = jnp.bitwise_xor(
            lookup(occ_irrep, piece_pairs // norb), lookup(occ_irrep, piece_pairs % norb)
        )
        masked_t = jnp.where(piece_irrep[:, None] == cd_irrep[None, :], panel, zero_half)
        terms.append(jnp.dot(masked_t, masked_v, preferred_element_type=jnp.float32))
    total = jnp.concatenate(terms, axis=0)
    ntiles = tile_owner.shape[0]
    tile_ids = jnp.arange(ntiles, dtype=jnp.int32)
    same = tile_owner[:, None] == tile_owner[None, :]
    earlier = tile_ids[:, None] > tile_ids[None, :]
    rank = jnp.sum(jnp.where(same & earlier, 1, 0), axis=1).astype(jnp.int32)
    slot = tile_owner * CAP + rank
    summed = lax.psum(total, ("row", "col"))
    wanted = myself * CAP + jnp.arange(CAP, dtype=jnp.int32)
    match = slot[None, :] == wanted[:, None]
    source = jnp.sum(jnp.where(match, tile_ids[None, :], 0), axis=1)
    found = jnp.any(match, axis=1)
    pair_rows = source[:, None] * TR + jnp.arange(TR, dtype=jnp.int32)[None, :]
    sender = pair_rows // local_pairs
    within = pair_rows % local_pairs
    which = (within // rows_piece).reshape(CAP * TR)
    rows = (sender * rows_piece + within % rows_piece).reshape(CAP * TR)
    keep = jnp.repeat(found, TR)
    flat_rows = which * (ncols * rows_piece) + rows
    summed = summed.reshape(PIECES * ncols * rows_piece, ab_width)
    picked = jnp.take(summed, flat_rows, axis=0).astype(jnp.bfloat16)
    placed = jnp.where(keep[:, None], picked, zero_half)
    return placed.reshape(CAP * TR, ab_width)


def solution(mesh):
    in_specs = (P("col", "row"), P(("row", "col"), None), P(), P(), P())
    out_specs = P(("row", "col"), None)
    return jax.shard_map(
        on_device, mesh=mesh, in_specs=in_specs, out_specs=out_specs, check_vma=False
    )
```

```python
import jax
import jax.numpy as jnp
from jax import lax
from jax.sharding import PartitionSpec as P

TR = 2
TILES_DEV = 3
CAP = 6
PIECES = 2


def lookup(table, index):
    levels = jnp.arange(1, 8, dtype=jnp.int32)
    starts = jnp.sum((table[None, :] < levels[:, None]).astype(jnp.int32), axis=1)
    return jnp.sum((index[:, None] >= starts[None, :]).astype(jnp.int32), axis=1)


def on_device(amplitudes, integrals, occ_irrep, vir_irrep, tile_owner):
    ncols = lax.axis_size("col")
    nrows = lax.axis_size("row")
    myself = lax.axis_index("row") * ncols + lax.axis_index("col")
    cd_dev = integrals.shape[0]
    ab_width = integrals.shape[1]
    local_pairs = amplitudes.shape[0]
    norb = occ_irrep.shape[0]
    nvirt = vir_irrep.shape[0]
    ab_index = jnp.arange(ab_width, dtype=jnp.int32)
    ab_irrep = jnp.bitwise_xor(
        lookup(vir_irrep, ab_index // nvirt), lookup(vir_irrep, ab_index % nvirt)
    )
    zero_half = jnp.zeros((), jnp.bfloat16)
    cd_index = myself * cd_dev + jnp.arange(cd_dev, dtype=jnp.int32)
    cd_irrep = jnp.bitwise_xor(
        lookup(vir_irrep, cd_index // nvirt), lookup(vir_irrep, cd_index % nvirt)
    )
    masked_v = jnp.where(cd_irrep[:, None] == ab_irrep[None, :], integrals, zero_half)
    rows_piece = local_pairs // PIECES
    terms = []
    for h in range(PIECES):
        part = amplitudes[h * rows_piece:(h + 1) * rows_piece]
        panel = lax.all_to_all(part, "col", split_axis=1, concat_axis=0, tiled=True)
        piece_pairs = (
            jnp.arange(ncols, dtype=jnp.int32)[:, None] * local_pairs
            + h * rows_piece
            + jnp.arange(rows_piece, dtype=jnp.int32)[None, :]
        ).reshape(ncols * rows_piece)
        piece_irrep = jnp.bitwise_xor(
            lookup(occ_irrep, piece_pairs // norb), lookup(occ_irrep, piece_pairs % norb)
        )
        masked_t = jnp.where(piece_irrep[:, None] == cd_irrep[None, :], panel, zero_half)
        term = jnp.dot(masked_t, masked_v, preferred_element_type=jnp.float32)
        if terms:
            terms[-1], term = lax.optimization_barrier((terms[-1], term))
        terms.append(lax.psum(term, ("row", "col")))
    summed = jnp.concatenate(terms, axis=0)
    ntiles = tile_owner.shape[0]
    tile_ids = jnp.arange(ntiles, dtype=jnp.int32)
    same = tile_owner[:, None] == tile_owner[None, :]
    earlier = tile_ids[:, None] > tile_ids[None, :]
    rank = jnp.sum(jnp.where(same & earlier, 1, 0), axis=1).astype(jnp.int32)
    slot = tile_owner * CAP + rank
    wanted = myself * CAP + jnp.arange(CAP, dtype=jnp.int32)
    match = slot[None, :] == wanted[:, None]
    source = jnp.sum(jnp.where(match, tile_ids[None, :], 0), axis=1)
    found = jnp.any(match, axis=1)
    pair_rows = source[:, None] * TR + jnp.arange(TR, dtype=jnp.int32)[None, :]
    sender = pair_rows // local_pairs
    within = pair_rows % local_pairs
    which = (within // rows_piece).reshape(CAP * TR)
    rows = (sender * rows_piece + within % rows_piece).reshape(CAP * TR)
    keep = jnp.repeat(found, TR)
    flat_rows = which * (ncols * rows_piece) + rows
    summed = summed.reshape(PIECES * ncols * rows_piece, ab_width)
    picked = jnp.take(summed, flat_rows, axis=0).astype(jnp.bfloat16)
    placed = jnp.where(keep[:, None], picked, zero_half)
    return placed.reshape(CAP * TR, ab_width)


def solution(mesh):
    in_specs = (P("col", "row"), P(("row", "col"), None), P(), P(), P())
    out_specs = P(("row", "col"), None)
    return jax.shard_map(
        on_device, mesh=mesh, in_specs=in_specs, out_specs=out_specs, check_vma=False
    )
```

```python
import jax
import jax.numpy as jnp
from jax import lax
from jax.sharding import PartitionSpec as P

TR = 2
TILES_DEV = 3
CAP = 6
PIECES = 3


def lookup(table, index):
    levels = jnp.arange(1, 8, dtype=jnp.int32)
    starts = jnp.sum((table[None, :] < levels[:, None]).astype(jnp.int32), axis=1)
    return jnp.sum((index[:, None] >= starts[None, :]).astype(jnp.int32), axis=1)


def on_device(amplitudes, integrals, occ_irrep, vir_irrep, tile_owner):
    ncols = lax.axis_size("col")
    nrows = lax.axis_size("row")
    myself = lax.axis_index("row") * ncols + lax.axis_index("col")
    cd_dev = integrals.shape[0]
    ab_width = integrals.shape[1]
    local_pairs = amplitudes.shape[0]
    norb = occ_irrep.shape[0]
    nvirt = vir_irrep.shape[0]
    ab_index = jnp.arange(ab_width, dtype=jnp.int32)
    ab_irrep = jnp.bitwise_xor(
        lookup(vir_irrep, ab_index // nvirt), lookup(vir_irrep, ab_index % nvirt)
    )
    zero_half = jnp.zeros((), jnp.bfloat16)
    cd_index = myself * cd_dev + jnp.arange(cd_dev, dtype=jnp.int32)
    cd_irrep = jnp.bitwise_xor(
        lookup(vir_irrep, cd_index // nvirt), lookup(vir_irrep, cd_index % nvirt)
    )
    masked_v = jnp.where(cd_irrep[:, None] == ab_irrep[None, :], integrals, zero_half)
    rows_piece = local_pairs // PIECES
    terms = []
    for h in range(PIECES):
        part = jnp.transpose(
            amplitudes[h * rows_piece:(h + 1) * rows_piece].reshape(rows_piece, ncols, cd_dev),
            (1, 0, 2),
        )
        panel = lax.all_to_all(part, "col", split_axis=0, concat_axis=0, tiled=True)
        panel = panel.reshape(ncols * rows_piece, cd_dev)
        piece_pairs = (
            jnp.arange(ncols, dtype=jnp.int32)[:, None] * local_pairs
            + h * rows_piece
            + jnp.arange(rows_piece, dtype=jnp.int32)[None, :]
        ).reshape(ncols * rows_piece)
        piece_irrep = jnp.bitwise_xor(
            lookup(occ_irrep, piece_pairs // norb), lookup(occ_irrep, piece_pairs % norb)
        )
        masked_t = jnp.where(piece_irrep[:, None] == cd_irrep[None, :], panel, zero_half)
        terms.append(jnp.dot(masked_t, masked_v, preferred_element_type=jnp.float32))
    total = jnp.concatenate(terms, axis=0)
    ntiles = tile_owner.shape[0]
    tile_ids = jnp.arange(ntiles, dtype=jnp.int32)
    same = tile_owner[:, None] == tile_owner[None, :]
    earlier = tile_ids[:, None] > tile_ids[None, :]
    rank = jnp.sum(jnp.where(same & earlier, 1, 0), axis=1).astype(jnp.int32)
    slot = tile_owner * CAP + rank
    summed = lax.psum(total, ("row", "col"))
    wanted = myself * CAP + jnp.arange(CAP, dtype=jnp.int32)
    match = slot[None, :] == wanted[:, None]
    source = jnp.sum(jnp.where(match, tile_ids[None, :], 0), axis=1)
    found = jnp.any(match, axis=1)
    pair_rows = source[:, None] * TR + jnp.arange(TR, dtype=jnp.int32)[None, :]
    sender = pair_rows // local_pairs
    within = pair_rows % local_pairs
    which = (within // rows_piece).reshape(CAP * TR)
    rows = (sender * rows_piece + within % rows_piece).reshape(CAP * TR)
    keep = jnp.repeat(found, TR)
    flat_rows = which * (ncols * rows_piece) + rows
    summed = summed.reshape(PIECES * ncols * rows_piece, ab_width)
    starts = flat_rows.reshape(CAP, TR)[:, 0]
    picked = jnp.concatenate(
        [lax.dynamic_slice_in_dim(summed, starts[k], TR, axis=0) for k in range(CAP)], axis=0
    ).astype(jnp.bfloat16)
    placed = jnp.where(keep[:, None], picked, zero_half)
    return placed.reshape(CAP * TR, ab_width)


def solution(mesh):
    in_specs = (P("col", "row"), P(("row", "col"), None), P(), P(), P())
    out_specs = P(("row", "col"), None)
    return jax.shard_map(
        on_device, mesh=mesh, in_specs=in_specs, out_specs=out_specs, check_vma=False
    )
```

```python
import jax
import jax.numpy as jnp
from jax import lax
from jax.sharding import PartitionSpec as P

TR = 2
TILES_DEV = 3
CAP = 6
PIECES = 2


def lookup(table, index):
    levels = jnp.arange(1, 8, dtype=jnp.int32)
    starts = jnp.sum((table[None, :] < levels[:, None]).astype(jnp.int32), axis=1)
    return jnp.sum((index[:, None] >= starts[None, :]).astype(jnp.int32), axis=1)


def on_device(amplitudes, integrals, occ_irrep, vir_irrep, tile_owner):
    ncols = lax.axis_size("col")
    nrows = lax.axis_size("row")
    myself = lax.axis_index("row") * ncols + lax.axis_index("col")
    cd_dev = integrals.shape[0]
    ab_width = integrals.shape[1]
    local_pairs = amplitudes.shape[0]
    norb = occ_irrep.shape[0]
    nvirt = vir_irrep.shape[0]
    ab_index = jnp.arange(ab_width, dtype=jnp.int32)
    ab_irrep = jnp.bitwise_xor(
        lookup(vir_irrep, ab_index // nvirt), lookup(vir_irrep, ab_index % nvirt)
    )
    zero_half = jnp.zeros((), jnp.bfloat16)
    cd_index = myself * cd_dev + jnp.arange(cd_dev, dtype=jnp.int32)
    cd_irrep = jnp.bitwise_xor(
        lookup(vir_irrep, cd_index // nvirt), lookup(vir_irrep, cd_index % nvirt)
    )
    masked_v = jnp.where(cd_irrep[:, None] == ab_irrep[None, :], integrals, zero_half)
    rows_piece = local_pairs // PIECES
    terms = []
    stacked = amplitudes.reshape(PIECES, rows_piece, ncols * cd_dev)
    for h in range(PIECES):
        part = jnp.transpose(
            stacked[h].reshape(rows_piece, ncols, cd_dev),
            (1, 0, 2),
        )
        panel = lax.all_to_all(part, "col", split_axis=0, concat_axis=0, tiled=True)
        panel = panel.reshape(ncols * rows_piece, cd_dev)
        piece_pairs = (
            jnp.arange(ncols, dtype=jnp.int32)[:, None] * local_pairs
            + h * rows_piece
            + jnp.arange(rows_piece, dtype=jnp.int32)[None, :]
        ).reshape(ncols * rows_piece)
        piece_irrep = jnp.bitwise_xor(
            lookup(occ_irrep, piece_pairs // norb), lookup(occ_irrep, piece_pairs % norb)
        )
        masked_t = jnp.where(piece_irrep[:, None] == cd_irrep[None, :], panel, zero_half)
        terms.append(jnp.dot(masked_t, masked_v, preferred_element_type=jnp.float32))
    total = jnp.concatenate(terms, axis=0)
    ntiles = tile_owner.shape[0]
    tile_ids = jnp.arange(ntiles, dtype=jnp.int32)
    same = tile_owner[:, None] == tile_owner[None, :]
    earlier = tile_ids[:, None] > tile_ids[None, :]
    rank = jnp.sum(jnp.where(same & earlier, 1, 0), axis=1).astype(jnp.int32)
    slot = tile_owner * CAP + rank
    summed = lax.psum(total, ("row", "col"))
    wanted = myself * CAP + jnp.arange(CAP, dtype=jnp.int32)
    match = slot[None, :] == wanted[:, None]
    source = jnp.sum(jnp.where(match, tile_ids[None, :], 0), axis=1)
    found = jnp.any(match, axis=1)
    pair_rows = source[:, None] * TR + jnp.arange(TR, dtype=jnp.int32)[None, :]
    sender = pair_rows // local_pairs
    within = pair_rows % local_pairs
    which = (within // rows_piece).reshape(CAP * TR)
    rows = (sender * rows_piece + within % rows_piece).reshape(CAP * TR)
    keep = jnp.repeat(found, TR)
    flat_rows = which * (ncols * rows_piece) + rows
    summed = summed.reshape(PIECES * ncols * rows_piece, ab_width)
    starts = flat_rows.reshape(CAP, TR)[:, 0]
    picked = jnp.concatenate(
        [lax.dynamic_slice_in_dim(summed, starts[k], TR, axis=0) for k in range(CAP)], axis=0
    ).astype(jnp.bfloat16)
    placed = jnp.where(keep[:, None], picked, zero_half)
    return placed.reshape(CAP * TR, ab_width)


def solution(mesh):
    in_specs = (P("col", "row"), P(("row", "col"), None), P(), P(), P())
    out_specs = P(("row", "col"), None)
    return jax.shard_map(
        on_device, mesh=mesh, in_specs=in_specs, out_specs=out_specs, check_vma=False
    )
```

```python
import jax
import jax.numpy as jnp
from jax import lax
from jax.sharding import PartitionSpec as P

TR = 2
TILES_DEV = 3
CAP = 6
FIRST_ROWS = 8


def lookup(table, index):
    levels = jnp.arange(1, 8, dtype=jnp.int32)
    starts = jnp.sum((table[None, :] < levels[:, None]).astype(jnp.int32), axis=1)
    return jnp.sum((index[:, None] >= starts[None, :]).astype(jnp.int32), axis=1)


def on_device(amplitudes, integrals, occ_irrep, vir_irrep, tile_owner):
    ncols = lax.axis_size("col")
    nrows = lax.axis_size("row")
    myself = lax.axis_index("row") * ncols + lax.axis_index("col")
    cd_dev = integrals.shape[0]
    ab_width = integrals.shape[1]
    local_pairs = amplitudes.shape[0]
    norb = occ_irrep.shape[0]
    nvirt = vir_irrep.shape[0]
    ab_index = jnp.arange(ab_width, dtype=jnp.int32)
    ab_irrep = jnp.bitwise_xor(
        lookup(vir_irrep, ab_index // nvirt), lookup(vir_irrep, ab_index % nvirt)
    )
    zero_half = jnp.zeros((), jnp.bfloat16)
    cd_index = myself * cd_dev + jnp.arange(cd_dev, dtype=jnp.int32)
    cd_irrep = jnp.bitwise_xor(
        lookup(vir_irrep, cd_index // nvirt), lookup(vir_irrep, cd_index % nvirt)
    )
    masked_v = jnp.where(cd_irrep[:, None] == ab_irrep[None, :], integrals, zero_half)
    cuts = [0, FIRST_ROWS, local_pairs]
    terms = []
    for h in range(len(cuts) - 1):
        lo, rows_piece = cuts[h], cuts[h + 1] - cuts[h]
        part = jnp.transpose(
            amplitudes[lo:lo + rows_piece].reshape(rows_piece, ncols, cd_dev),
            (1, 0, 2),
        )
        panel = lax.all_to_all(part, "col", split_axis=0, concat_axis=0, tiled=True)
        panel = panel.reshape(ncols * rows_piece, cd_dev)
        piece_pairs = (
            jnp.arange(ncols, dtype=jnp.int32)[:, None] * local_pairs
            + lo
            + jnp.arange(rows_piece, dtype=jnp.int32)[None, :]
        ).reshape(ncols * rows_piece)
        piece_irrep = jnp.bitwise_xor(
            lookup(occ_irrep, piece_pairs // norb), lookup(occ_irrep, piece_pairs % norb)
        )
        masked_t = jnp.where(piece_irrep[:, None] == cd_irrep[None, :], panel, zero_half)
        terms.append(jnp.dot(masked_t, masked_v, preferred_element_type=jnp.float32))
    total = jnp.concatenate(terms, axis=0)
    ntiles = tile_owner.shape[0]
    tile_ids = jnp.arange(ntiles, dtype=jnp.int32)
    same = tile_owner[:, None] == tile_owner[None, :]
    earlier = tile_ids[:, None] > tile_ids[None, :]
    rank = jnp.sum(jnp.where(same & earlier, 1, 0), axis=1).astype(jnp.int32)
    slot = tile_owner * CAP + rank
    summed = lax.psum(total, ("row", "col"))
    wanted = myself * CAP + jnp.arange(CAP, dtype=jnp.int32)
    match = slot[None, :] == wanted[:, None]
    source = jnp.sum(jnp.where(match, tile_ids[None, :], 0), axis=1)
    found = jnp.any(match, axis=1)
    pair_rows = source[:, None] * TR + jnp.arange(TR, dtype=jnp.int32)[None, :]
    sender = pair_rows // local_pairs
    within = pair_rows % local_pairs
    late = within >= FIRST_ROWS
    flat_rows = jnp.where(
        late,
        ncols * FIRST_ROWS + sender * (local_pairs - FIRST_ROWS) + within - FIRST_ROWS,
        sender * FIRST_ROWS + within,
    ).reshape(CAP * TR)
    keep = jnp.repeat(found, TR)
    starts = flat_rows.reshape(CAP, TR)[:, 0]
    picked = jnp.concatenate(
        [lax.dynamic_slice_in_dim(summed, starts[k], TR, axis=0) for k in range(CAP)], axis=0
    ).astype(jnp.bfloat16)
    placed = jnp.where(keep[:, None], picked, zero_half)
    return placed.reshape(CAP * TR, ab_width)


def solution(mesh):
    in_specs = (P("col", "row"), P(("row", "col"), None), P(), P(), P())
    out_specs = P(("row", "col"), None)
    return jax.shard_map(
        on_device, mesh=mesh, in_specs=in_specs, out_specs=out_specs, check_vma=False
    )
```

```python
import jax
import jax.numpy as jnp
from jax import lax
from jax.sharding import PartitionSpec as P

TR = 2
TILES_DEV = 3
CAP = 6
PIECES = 2


def lookup(table, index):
    levels = jnp.arange(1, 8, dtype=jnp.int32)
    starts = jnp.sum((table[None, :] < levels[:, None]).astype(jnp.int32), axis=1)
    return jnp.sum((index[:, None] >= starts[None, :]).astype(jnp.int32), axis=1)


def on_device(amplitudes, integrals, occ_irrep, vir_irrep, tile_owner):
    ncols = lax.axis_size("col")
    nrows = lax.axis_size("row")
    myself = lax.axis_index("row") * ncols + lax.axis_index("col")
    cd_dev = integrals.shape[0]
    ab_width = integrals.shape[1]
    local_pairs = amplitudes.shape[0]
    norb = occ_irrep.shape[0]
    nvirt = vir_irrep.shape[0]
    ab_index = jnp.arange(ab_width, dtype=jnp.int32)
    ab_irrep = jnp.bitwise_xor(
        lookup(vir_irrep, ab_index // nvirt), lookup(vir_irrep, ab_index % nvirt)
    )
    zero_half = jnp.zeros((), jnp.bfloat16)
    cd_index = myself * cd_dev + jnp.arange(cd_dev, dtype=jnp.int32)
    cd_irrep = jnp.bitwise_xor(
        lookup(vir_irrep, cd_index // nvirt), lookup(vir_irrep, cd_index % nvirt)
    )
    masked_v = jnp.where(cd_irrep[:, None] == ab_irrep[None, :], integrals, zero_half)
    rows_piece = local_pairs // PIECES
    terms = []
    source_rows = amplitudes
    for h in range(PIECES):
        rows_h = source_rows[h * rows_piece:(h + 1) * rows_piece]
        part = jnp.transpose(rows_h.reshape(rows_piece, ncols, cd_dev), (1, 0, 2))
        source_rows, part = lax.optimization_barrier((source_rows, part))
        panel = lax.all_to_all(part, "col", split_axis=0, concat_axis=0, tiled=True)
        panel = panel.reshape(ncols * rows_piece, cd_dev)
        piece_pairs = (
            jnp.arange(ncols, dtype=jnp.int32)[:, None] * local_pairs
            + h * rows_piece
            + jnp.arange(rows_piece, dtype=jnp.int32)[None, :]
        ).reshape(ncols * rows_piece)
        piece_irrep = jnp.bitwise_xor(
            lookup(occ_irrep, piece_pairs // norb), lookup(occ_irrep, piece_pairs % norb)
        )
        masked_t = jnp.where(piece_irrep[:, None] == cd_irrep[None, :], panel, zero_half)
        terms.append(jnp.dot(masked_t, masked_v, preferred_element_type=jnp.float32))
    ntiles = tile_owner.shape[0]
    tile_ids = jnp.arange(ntiles, dtype=jnp.int32)
    same = tile_owner[:, None] == tile_owner[None, :]
    earlier = tile_ids[:, None] > tile_ids[None, :]
    rank = jnp.sum(jnp.where(same & earlier, 1, 0), axis=1).astype(jnp.int32)
    slot = tile_owner * CAP + rank
    summed = lax.psum(tuple(terms), ("row", "col"))
    wanted = myself * CAP + jnp.arange(CAP, dtype=jnp.int32)
    match = slot[None, :] == wanted[:, None]
    source = jnp.sum(jnp.where(match, tile_ids[None, :], 0), axis=1)
    found = jnp.any(match, axis=1)
    pair_rows = source[:, None] * TR + jnp.arange(TR, dtype=jnp.int32)[None, :]
    sender = pair_rows // local_pairs
    within = pair_rows % local_pairs
    which = (within // rows_piece).reshape(CAP * TR)
    rows = (sender * rows_piece + within % rows_piece).reshape(CAP * TR)
    keep = jnp.repeat(found, TR)
    which = which.reshape(CAP, TR)[:, 0]
    starts = rows.reshape(CAP, TR)[:, 0]
    pieces = []
    for k in range(CAP):
        options = [lax.dynamic_slice_in_dim(s, starts[k], TR, axis=0) for s in summed]
        chosen = options[0]
        for h in range(1, PIECES):
            chosen = jnp.where(which[k] == h, options[h], chosen)
        pieces.append(chosen)
    picked = jnp.concatenate(pieces, axis=0).astype(jnp.bfloat16)
    placed = jnp.where(keep[:, None], picked, zero_half)
    return placed.reshape(CAP * TR, ab_width)


def solution(mesh):
    in_specs = (P("col", "row"), P(("row", "col"), None), P(), P(), P())
    out_specs = P(("row", "col"), None)
    return jax.shard_map(
        on_device, mesh=mesh, in_specs=in_specs, out_specs=out_specs, check_vma=False
    )
```

```python
import jax
import jax.numpy as jnp
from jax import lax
from jax.sharding import PartitionSpec as P

TR = 2
TILES_DEV = 3
CAP = 6
PIECES = 2


def lookup(table, index):
    levels = jnp.arange(1, 8, dtype=jnp.int32)
    starts = jnp.sum((table[None, :] < levels[:, None]).astype(jnp.int32), axis=1)
    return jnp.sum((index[:, None] >= starts[None, :]).astype(jnp.int32), axis=1)


def on_device(amplitudes, integrals, occ_irrep, vir_irrep, tile_owner):
    ncols = lax.axis_size("col")
    nrows = lax.axis_size("row")
    myself = lax.axis_index("row") * ncols + lax.axis_index("col")
    cd_dev = integrals.shape[0]
    ab_width = integrals.shape[1]
    local_pairs = amplitudes.shape[0]
    norb = occ_irrep.shape[0]
    nvirt = vir_irrep.shape[0]
    ab_index = jnp.arange(ab_width, dtype=jnp.int32)
    ab_irrep = jnp.bitwise_xor(
        lookup(vir_irrep, ab_index // nvirt), lookup(vir_irrep, ab_index % nvirt)
    )
    zero_half = jnp.zeros((), jnp.bfloat16)
    cd_index = myself * cd_dev + jnp.arange(cd_dev, dtype=jnp.int32)
    cd_irrep = jnp.bitwise_xor(
        lookup(vir_irrep, cd_index // nvirt), lookup(vir_irrep, cd_index % nvirt)
    )
    masked_v = jnp.where(cd_irrep[:, None] == ab_irrep[None, :], integrals, zero_half)
    rows_piece = local_pairs // PIECES
    terms = []
    source_rows = amplitudes
    for h in range(PIECES):
        rows_h = source_rows[h * rows_piece:(h + 1) * rows_piece]
        part = jnp.transpose(rows_h.reshape(rows_piece, ncols, cd_dev), (1, 0, 2))
        source_rows, part = lax.optimization_barrier((source_rows, part))
        panel = lax.all_to_all(part, "col", split_axis=0, concat_axis=0, tiled=True)
        panel = panel.reshape(ncols * rows_piece, cd_dev)
        piece_pairs = (
            jnp.arange(ncols, dtype=jnp.int32)[:, None] * local_pairs
            + h * rows_piece
            + jnp.arange(rows_piece, dtype=jnp.int32)[None, :]
        ).reshape(ncols * rows_piece)
        piece_irrep = jnp.bitwise_xor(
            lookup(occ_irrep, piece_pairs // norb), lookup(occ_irrep, piece_pairs % norb)
        )
        masked_t = jnp.where(piece_irrep[:, None] == cd_irrep[None, :], panel, zero_half)
        terms.append(jnp.dot(masked_t, masked_v, preferred_element_type=jnp.float32))
    ntiles = tile_owner.shape[0]
    tile_ids = jnp.arange(ntiles, dtype=jnp.int32)
    same = tile_owner[:, None] == tile_owner[None, :]
    earlier = tile_ids[:, None] > tile_ids[None, :]
    rank = jnp.sum(jnp.where(same & earlier, 1, 0), axis=1).astype(jnp.int32)
    slot = tile_owner * CAP + rank
    summed = lax.psum(tuple(terms), ("row", "col"))
    wanted = myself * CAP + jnp.arange(CAP, dtype=jnp.int32)
    match = slot[None, :] == wanted[:, None]
    source = jnp.sum(jnp.where(match, tile_ids[None, :], 0), axis=1)
    found = jnp.any(match, axis=1)
    pair_rows = source[:, None] * TR + jnp.arange(TR, dtype=jnp.int32)[None, :]
    sender = pair_rows // local_pairs
    within = pair_rows % local_pairs
    which = (within // rows_piece).reshape(CAP * TR)
    rows = (sender * rows_piece + within % rows_piece).reshape(CAP * TR)
    keep = jnp.repeat(found, TR)
    picked = None
    for h in range(PIECES):
        hits = (which == h)[:, None] & (
            rows[:, None] == jnp.arange(summed[h].shape[0], dtype=jnp.int32)[None, :]
        )
        picker = hits.astype(summed[h].dtype)
        term = jnp.dot(picker, summed[h], preferred_element_type=jnp.float32)
        picked = term if picked is None else picked + term
    picked = picked.astype(jnp.bfloat16)
    placed = jnp.where(keep[:, None], picked, zero_half)
    return placed.reshape(CAP * TR, ab_width)


def solution(mesh):
    in_specs = (P("col", "row"), P(("row", "col"), None), P(), P(), P())
    out_specs = P(("row", "col"), None)
    return jax.shard_map(
        on_device, mesh=mesh, in_specs=in_specs, out_specs=out_specs, check_vma=False
    )
```

```python
import jax
import jax.numpy as jnp
from jax import lax
from jax.sharding import PartitionSpec as P

TR = 2
TILES_DEV = 3
CAP = 6
PIECES = 2


def lookup(table, index):
    levels = jnp.arange(1, 8, dtype=jnp.int32)
    starts = jnp.sum((table[None, :] < levels[:, None]).astype(jnp.int32), axis=1)
    return jnp.sum((index[:, None] >= starts[None, :]).astype(jnp.int32), axis=1)


def on_device(amplitudes, integrals, occ_irrep, vir_irrep, tile_owner):
    ncols = lax.axis_size("col")
    nrows = lax.axis_size("row")
    myself = lax.axis_index("row") * ncols + lax.axis_index("col")
    cd_dev = integrals.shape[0]
    ab_width = integrals.shape[1]
    local_pairs = amplitudes.shape[0]
    norb = occ_irrep.shape[0]
    nvirt = vir_irrep.shape[0]
    ab_index = jnp.arange(ab_width, dtype=jnp.int32)
    ab_irrep = jnp.bitwise_xor(
        lookup(vir_irrep, ab_index // nvirt), lookup(vir_irrep, ab_index % nvirt)
    )
    zero_half = jnp.zeros((), jnp.bfloat16)
    cd_index = myself * cd_dev + jnp.arange(cd_dev, dtype=jnp.int32)
    cd_irrep = jnp.bitwise_xor(
        lookup(vir_irrep, cd_index // nvirt), lookup(vir_irrep, cd_index % nvirt)
    )
    masked_v = jnp.where(cd_irrep[:, None] == ab_irrep[None, :], integrals, zero_half)
    masked_v = lax.optimization_barrier(masked_v)
    rows_piece = local_pairs // PIECES
    terms = []
    source_rows = amplitudes
    for h in range(PIECES):
        rows_h = source_rows[h * rows_piece:(h + 1) * rows_piece]
        part = jnp.transpose(rows_h.reshape(rows_piece, ncols, cd_dev), (1, 0, 2))
        source_rows, part = lax.optimization_barrier((source_rows, part))
        panel = lax.all_to_all(part, "col", split_axis=0, concat_axis=0, tiled=True)
        panel = panel.reshape(ncols * rows_piece, cd_dev)
        piece_pairs = (
            jnp.arange(ncols, dtype=jnp.int32)[:, None] * local_pairs
            + h * rows_piece
            + jnp.arange(rows_piece, dtype=jnp.int32)[None, :]
        ).reshape(ncols * rows_piece)
        piece_irrep = jnp.bitwise_xor(
            lookup(occ_irrep, piece_pairs // norb), lookup(occ_irrep, piece_pairs % norb)
        )
        masked_t = jnp.where(piece_irrep[:, None] == cd_irrep[None, :], panel, zero_half)
        terms.append(jnp.dot(masked_t, masked_v, preferred_element_type=jnp.float32))
    ntiles = tile_owner.shape[0]
    tile_ids = jnp.arange(ntiles, dtype=jnp.int32)
    same = tile_owner[:, None] == tile_owner[None, :]
    earlier = tile_ids[:, None] > tile_ids[None, :]
    rank = jnp.sum(jnp.where(same & earlier, 1, 0), axis=1).astype(jnp.int32)
    slot = tile_owner * CAP + rank
    summed = lax.psum(tuple(terms), ("row", "col"))
    wanted = myself * CAP + jnp.arange(CAP, dtype=jnp.int32)
    match = slot[None, :] == wanted[:, None]
    source = jnp.sum(jnp.where(match, tile_ids[None, :], 0), axis=1)
    found = jnp.any(match, axis=1)
    pair_rows = source[:, None] * TR + jnp.arange(TR, dtype=jnp.int32)[None, :]
    sender = pair_rows // local_pairs
    within = pair_rows % local_pairs
    which = (within // rows_piece).reshape(CAP * TR)
    rows = (sender * rows_piece + within % rows_piece).reshape(CAP * TR)
    keep = jnp.repeat(found, TR)
    picked = None
    for h in range(PIECES):
        hits = (which == h)[:, None] & (
            rows[:, None] == jnp.arange(summed[h].shape[0], dtype=jnp.int32)[None, :]
        )
        picker = hits.astype(summed[h].dtype)
        term = jnp.dot(picker, summed[h], preferred_element_type=jnp.float32)
        picked = term if picked is None else picked + term
    picked = picked.astype(jnp.bfloat16)
    placed = jnp.where(keep[:, None], picked, zero_half)
    return placed.reshape(CAP * TR, ab_width)


def solution(mesh):
    in_specs = (P("col", "row"), P(("row", "col"), None), P(), P(), P())
    out_specs = P(("row", "col"), None)
    return jax.shard_map(
        on_device, mesh=mesh, in_specs=in_specs, out_specs=out_specs, check_vma=False
    )
```

```python
import jax
import jax.numpy as jnp
from jax import lax
from jax.sharding import PartitionSpec as P

TR = 2
TILES_DEV = 3
CAP = 6
PIECES = 2


def lookup(table, index):
    levels = jnp.arange(1, 8, dtype=jnp.int32)
    starts = jnp.sum((table[None, :] < levels[:, None]).astype(jnp.int32), axis=1)
    return jnp.sum((index[:, None] >= starts[None, :]).astype(jnp.int32), axis=1)


def on_device(amplitudes, integrals, occ_irrep, vir_irrep, tile_owner):
    ncols = lax.axis_size("col")
    nrows = lax.axis_size("row")
    myself = lax.axis_index("row") * ncols + lax.axis_index("col")
    cd_dev = integrals.shape[0]
    ab_width = integrals.shape[1]
    local_pairs = amplitudes.shape[0]
    norb = occ_irrep.shape[0]
    nvirt = vir_irrep.shape[0]
    ab_index = jnp.arange(ab_width, dtype=jnp.int32)
    ab_irrep = jnp.bitwise_xor(
        lookup(vir_irrep, ab_index // nvirt), lookup(vir_irrep, ab_index % nvirt)
    )
    zero_half = jnp.zeros((), jnp.bfloat16)
    cd_index = myself * cd_dev + jnp.arange(cd_dev, dtype=jnp.int32)
    cd_irrep = jnp.bitwise_xor(
        lookup(vir_irrep, cd_index // nvirt), lookup(vir_irrep, cd_index % nvirt)
    )
    masked_v = jnp.where(cd_irrep[:, None] == ab_irrep[None, :], integrals, zero_half)
    rows_piece = local_pairs // PIECES
    terms = []
    source_rows = amplitudes
    for h in range(PIECES):
        rows_h = source_rows[h * rows_piece:(h + 1) * rows_piece]
        part = jnp.transpose(rows_h.reshape(rows_piece, ncols, cd_dev), (1, 0, 2))
        source_rows, part = lax.optimization_barrier((source_rows, part))
        panel = lax.all_to_all(part, "col", split_axis=0, concat_axis=0, tiled=True)
        panel = panel.reshape(ncols * rows_piece, cd_dev)
        piece_pairs = (
            jnp.arange(ncols, dtype=jnp.int32)[:, None] * local_pairs
            + h * rows_piece
            + jnp.arange(rows_piece, dtype=jnp.int32)[None, :]
        ).reshape(ncols * rows_piece)
        piece_irrep = jnp.bitwise_xor(
            lookup(occ_irrep, piece_pairs // norb), lookup(occ_irrep, piece_pairs % norb)
        )
        masked_t = jnp.where(piece_irrep[:, None] == cd_irrep[None, :], panel, zero_half)
        terms.append(jnp.dot(masked_t, masked_v, preferred_element_type=jnp.float32))
    ntiles = tile_owner.shape[0]
    tile_ids = jnp.arange(ntiles, dtype=jnp.int32)
    same = tile_owner[:, None] == tile_owner[None, :]
    earlier = tile_ids[:, None] > tile_ids[None, :]
    rank = jnp.sum(jnp.where(same & earlier, 1, 0), axis=1).astype(jnp.int32)
    slot = tile_owner * CAP + rank
    summed = lax.psum(tuple(terms), ("row", "col"))
    wanted = myself * CAP + jnp.arange(CAP, dtype=jnp.int32)
    match = slot[None, :] == wanted[:, None]
    source = jnp.sum(jnp.where(match, tile_ids[None, :], 0), axis=1)
    found = jnp.any(match, axis=1)
    pair_rows = source[:, None] * TR + jnp.arange(TR, dtype=jnp.int32)[None, :]
    sender = pair_rows // local_pairs
    within = pair_rows % local_pairs
    which = (within // rows_piece).reshape(CAP * TR)
    rows = (sender * rows_piece + within % rows_piece).reshape(CAP * TR)
    keep = jnp.repeat(found, TR)
    picked = None
    for h in range(PIECES):
        hits = ((which == h) & keep)[:, None] & (
            rows[:, None] == jnp.arange(summed[h].shape[0], dtype=jnp.int32)[None, :]
        )
        picker = hits.astype(summed[h].dtype)
        term = jnp.dot(picker, summed[h], preferred_element_type=jnp.float32)
        picked = term if picked is None else picked + term
    picked = picked.astype(jnp.bfloat16)
    return picked.reshape(CAP * TR, ab_width)


def solution(mesh):
    in_specs = (P("col", "row"), P(("row", "col"), None), P(), P(), P())
    out_specs = P(("row", "col"), None)
    return jax.shard_map(
        on_device, mesh=mesh, in_specs=in_specs, out_specs=out_specs, check_vma=False
    )
```
